128 devices in a mesh: dp: 32 (over y, z, core), group: 4 (over x).
Axes of the slice: x: 4, y: 4, z: 4, core: 2. Of those that a mesh axis runs over, the one named last changes fastest.
Arguments:
- gradients: bfloat16 [128, 2, 2048, 512], P(('dp', 'group'))
- errors: float32 [128, 2, 2048, 512], P(('dp', 'group')), may hold values from -4 to 4
- warm_right: float32 [2, 512, 32], replicated, may hold values from -6 to 6
- norm_grads: float32 [128, 2, 2048], P(('dp', 'group'))
- norm_weights: float32 [2, 2048], replicated, may hold values from 0.5 to 1.5
- norm_moment: float32 [2, 2048], replicated, may hold values from -4 to 4
- owners: int32 [128], replicated, may hold values from 0 to 127, as said below
- slot_weights: bfloat16 [128, 2, 32, 512], P(('dp', 'group')), may hold values from -6 to 6
- slot_moment: float32 [128, 2, 32, 512], P(('dp', 'group')), may hold values from -4 to 4
Outputs:
- new_errors: float32 [128, 2, 2048, 512], P(('dp', 'group'))
- new_slot_moment: float32 [128, 2, 32, 512], P(('dp', 'group'))
- new_weights: bfloat16 [2, 2048, 512], replicated
- new_norm_weights: float32 [2, 2048], replicated
- new_norm_moment: float32 [2, 2048], replicated
The draws below stay inside these ranges and needn't reach their ends.
Inputs may be any that keep to these rules, and one draw needn't show every extreme that they name: `owners`: each replica owns at most 2 pieces and some replica owns exactly 2; a replica's pieces occupy its slots in increasing piece order, the other slots hold nothing that is read.
All inputs are finite; a program needn't handle non-finite values.
Results may differ from the reference program's by a relative error of at most 0.0004.
Values may be sent and summed in bfloat16 or wider, within the bound.
No kernel may reach another device: no remote copies, remote signals or barrier semaphores. Data moves between devices by JAX's collectives and lax.ppermute only.
A program may use at most 128 MiB of HBM per device.

```python
import jax
import jax.numpy as jnp
from jax import lax

DW = 2048
KV = 512
RANK = 32
SLOTS = 2
REPLICAS = 128
PIECES = 128
RB = 32


def draw_gradients(key, part):
    own_key = jax.random.fold_in(key, 12)
    own = jax.random.normal(own_key, (REPLICAS, 2, DW, KV), jnp.float32)
    values = own
    return jnp.clip(values, -12.0, 12.0).astype(jnp.bfloat16)


def draw_norm_grads(key, part):
    common_key = jax.random.fold_in(key, 21)
    own_key = jax.random.fold_in(key, 22)
    steps = jnp.arange(REPLICAS).astype(jnp.float32) / max(REPLICAS - 1, 1)
    rise = 1.0 + 2.0 * steps
    common = 2.0 * jax.random.normal(common_key, (2, DW), jnp.float32)
    own = 2.0 * jax.random.normal(own_key, (REPLICAS, 2, DW), jnp.float32)
    return jnp.clip(common[None] + own * rise[:, None, None], -40.0, 40.0)


def draw_owners(key, part):
    first_key = jax.random.fold_in(key, 31)
    rest_key = jax.random.fold_in(key, 32)
    order_key = jax.random.fold_in(key, 33)
    full_owner = jax.random.randint(first_key, (), 0, REPLICAS).astype(jnp.int32)
    rest = (jax.random.permutation(rest_key, (REPLICAS - 1) * SLOTS)[:PIECES - SLOTS] // SLOTS).astype(jnp.int32)
    rest = rest + (rest >= full_owner).astype(jnp.int32)
    owners_all = jnp.concatenate([full_owner * jnp.ones((SLOTS,), jnp.int32), rest])
    order = jax.random.permutation(order_key, PIECES)
    return owners_all[order].astype(jnp.int32)


def block_scale(key, dims, shards, least, high):
    loudness = 1.0
    for position, parts in shards:
        draws = jax.random.uniform(jax.random.fold_in(jax.random.fold_in(key, 6), position), (parts,), jnp.float32, least / len(shards), high / len(shards))
        loudness = loudness * jnp.repeat(jnp.exp(draws), dims[position] // parts).reshape((-1,) + (1,) * (len(dims) - 1 - position))
    return loudness


def noise(stream_key, extent, spread, most, shards=(), kind=jnp.bfloat16):
    values = jax.random.normal(stream_key, extent, jnp.float32) * spread
    if len(shards) > 0:
        values = block_scale(stream_key, extent, shards, -0.22, 0.18) * values
    return jnp.clip(values, min=-most, max=most).astype(kind)


def setup_inputs(seed: int = 0) -> dict:
    splits = jax.random.split(jax.random.key(seed), 10)
    return {
        "gradients": draw_gradients(jax.random.fold_in(splits[9], 71), 0),
        "errors": noise(splits[1], (REPLICAS, 2, DW, KV), 0.5, 4.0, ((0, 128),), jnp.float32),
        "warm_right": noise(splits[2], (2, KV, RANK), 1.0, 6.0, (), jnp.float32),
        "norm_grads": draw_norm_grads(jax.random.fold_in(splits[9], 71), 0),
        "norm_weights": jnp.clip(1.0 + 0.1 * jax.random.normal(splits[4], (2, DW), jnp.float32), 0.5, 1.5),
        "norm_moment": noise(splits[5], (2, DW), 0.5, 4.0, (), jnp.float32),
        "owners": draw_owners(jax.random.fold_in(splits[9], 71), 0),
        "slot_weights": noise(splits[7], (REPLICAS, SLOTS, RB, KV), 1.0, 6.0, ((0, 128),)),
        "slot_moment": noise(splits[8], (REPLICAS, SLOTS, RB, KV), 0.5, 4.0, ((0, 128),), jnp.float32),
    }


momentum_decay = 0.9
step_rate = 0.5

def orthonormal(factor):
    gram = jnp.einsum('...dr,...ds->...rs', factor, factor, precision=lax.Precision.HIGHEST)
    lower_factor = jnp.linalg.cholesky(gram)
    solved = jax.scipy.linalg.solve_triangular(lower_factor, jnp.swapaxes(factor, -1, -2), lower=True)
    return jnp.swapaxes(solved, -1, -2)

def reference(gradients, errors, warm_right, norm_grads, norm_weights, norm_moment, owners, slot_weights, slot_moment):
    replicas = gradients.shape[0]
    indices = jnp.arange(replicas, dtype=jnp.int32)

    def merged_at(index):
        return gradients[index].astype(jnp.float32) + errors[index]

    def sum_left(right_basis):

        def add_term(total, index):
            term = jnp.einsum('mdk,mkr->mdr', merged_at(index), right_basis, precision=lax.Precision.HIGHEST)
            return (total + term, None)
        start = jnp.zeros((2, DW, RANK), jnp.float32)
        return lax.scan(add_term, start, indices)[0]

    def sum_right(left_basis):

        def add_term(total, index):
            term = jnp.einsum('mdk,mdr->mkr', merged_at(index), left_basis, precision=lax.Precision.HIGHEST)
            return (total + term, None)
        start = jnp.zeros((2, KV, RANK), jnp.float32)
        return lax.scan(add_term, start, indices)[0]
    left_one = orthonormal(sum_left(warm_right))
    right_one = sum_right(left_one) / replicas
    left_two = orthonormal(sum_left(right_one))
    right_two = sum_right(left_two) / replicas
    update = jnp.einsum('mdr,mkr->mdk', left_two, right_two, precision=lax.Precision.HIGHEST)
    new_errors = lax.map(lambda index: merged_at(index) - update, indices)
    summed_norm = jnp.sum(norm_grads, axis=0)
    new_norm_moment = momentum_decay * norm_moment + summed_norm / replicas
    new_norm_weights = norm_weights - step_rate * new_norm_moment
    positions = jnp.arange(PIECES, dtype=jnp.int32)
    same_owner = owners[:, None] == owners[None, :]
    earlier = positions[:, None] < positions[None, :]
    slot_of = jnp.sum((same_owner & earlier).astype(jnp.int32), axis=0).astype(jnp.int32)
    pieces = update.reshape(PIECES, RB, KV)
    fresh = momentum_decay * slot_moment[owners, slot_of] + pieces
    new_slot_moment = slot_moment.at[owners, slot_of].set(fresh)
    rows_new = slot_weights[owners, slot_of].astype(jnp.float32) - step_rate * fresh
    new_weights = rows_new.astype(jnp.bfloat16).reshape(2, DW, KV)
    return (new_errors, new_slot_moment, new_weights, new_norm_weights, new_norm_moment)
```

```python
import jax
import jax.numpy as jnp
from jax import lax
from jax.sharding import PartitionSpec as P

momentum_decay = 0.9
step_rate = 0.5
HI = lax.Precision.HIGHEST


def pair_steps(dp_size, group_size):
    dp = lax.axis_index("dp")
    g = lax.axis_index("group")
    steps = []
    steps.append(("dp", [(i, i ^ 1) for i in range(dp_size)], dp & 1))
    steps.append(("group", [(i, i ^ 1) for i in range(group_size)], (g ^ (g // 2)) & 1))
    steps.append(("group", [(i, group_size - 1 - i) for i in range(group_size)], g // (group_size // 2)))
    z_size = 4
    y_size = dp_size // (2 * z_size)

    def dp_of(y, z, c):
        return (y * z_size + z) * 2 + c

    zc = (dp // 2) % z_size
    yc = dp // (2 * z_size)
    perm_z1, perm_z2, perm_y1, perm_y2 = [], [], [], []
    for y in range(y_size):
        for z in range(z_size):
            for c in range(2):
                src = dp_of(y, z, c)
                perm_z1.append((src, dp_of(y, z ^ 1, c)))
                perm_z2.append((src, dp_of(y, z_size - 1 - z, c)))
                perm_y1.append((src, dp_of(y ^ 1, z, c)))
                perm_y2.append((src, dp_of(y_size - 1 - y, z, c)))
    steps.append(("dp", perm_z1, (zc ^ (zc // 2)) & 1))
    steps.append(("dp", perm_z2, zc // (z_size // 2)))
    steps.append(("dp", perm_y1, (yc ^ (yc // 2)) & 1))
    steps.append(("dp", perm_y2, yc // (y_size // 2)))
    return steps


def sum_doubling(x, steps):
    for axis, perm, _ in steps:
        x = x + lax.ppermute(x, axis, perm)
    return x


def sum_halving(x, steps, extra=None):
    bits = []
    for axis, perm, bit in steps:
        half = x.shape[0] // 2
        keep = lax.dynamic_slice_in_dim(x, bit * half, half)
        send = lax.dynamic_slice_in_dim(x, (1 - bit) * half, half)
        if extra is None:
            got = lax.ppermute(send, axis, perm)
        else:
            got, got_extra = lax.ppermute((send, extra), axis, perm)
            extra = extra + got_extra
        x = keep + got
        bits.append(bit)
    for (axis, perm, _), bit in zip(reversed(steps), reversed(bits)):
        got = lax.ppermute(x, axis, perm)
        low = jnp.where(bit == 0, x, got)
        high = jnp.where(bit == 0, got, x)
        x = jnp.concatenate([low, high])
    return x, extra


def orth_t(ft):
    gram = jnp.einsum("mrd,msd->mrs", ft, ft, precision=HI)
    lower_factor = jnp.linalg.cholesky(gram)
    return jax.scipy.linalg.solve_triangular(lower_factor, ft, lower=True)


def left_t(merged, right_t):
    return jnp.einsum("mdk,mrk->mrd", merged, right_t, precision=HI)


def right_t_of(merged, left_tr):
    return jnp.einsum("mdk,mrd->mrk", merged, left_tr, precision=HI)


def on_device(
    gradients,
    errors,
    warm_right,
    norm_grads,
    norm_weights,
    norm_moment,
    owners,
    slot_weights,
    slot_moment,
):
    dp_size = lax.axis_size("dp")
    group_size = lax.axis_size("group")
    replicas = dp_size * group_size
    steps = pair_steps(dp_size, group_size)
    merged = gradients[0].astype(jnp.float32) + errors[0]
    lshape = (merged.shape[0], warm_right.shape[2], merged.shape[1])

    p1 = left_t(merged, jnp.swapaxes(warm_right, 1, 2))
    p1_sum, norm_sum = sum_halving(p1.reshape(-1), steps, norm_grads[0])
    left_one = orth_t(p1_sum.reshape(lshape))
    right_one = sum_doubling(right_t_of(merged, left_one), steps) / replicas
    p2_sum, _ = sum_halving(left_t(merged, right_one).reshape(-1), steps)
    left_two = orth_t(p2_sum.reshape(lshape))
    right_two = sum_doubling(right_t_of(merged, left_two), steps) / replicas
    update = jnp.einsum("mrd,mrk->mdk", left_two, right_two, precision=HI)
    new_errors = (merged - update)[None]
    new_norm_moment = momentum_decay * norm_moment + norm_sum / replicas
    new_norm_weights = norm_weights - step_rate * new_norm_moment
    piece_count = owners.shape[0]
    slot_count = slot_moment.shape[1]
    piece_rows = slot_moment.shape[2]
    features = slot_moment.shape[3]
    positions = jnp.arange(piece_count, dtype=jnp.int32)
    same_owner = owners[:, None] == owners[None, :]
    earlier = positions[:, None] < positions[None, :]
    slot_of = jnp.sum((same_owner & earlier).astype(jnp.int32), axis=0)
    my_index = lax.axis_index(("dp", "group"))
    owned = owners == my_index
    slot_range = jnp.arange(slot_count, dtype=jnp.int32)
    selector = (owned[:, None] & (slot_of[:, None] == slot_range[None, :])).astype(jnp.float32)
    pieces = update.reshape(piece_count, piece_rows, features)
    slot_update = jnp.einsum("js,jrk->srk", selector, pieces, precision=HI)
    used = jnp.sum(selector, axis=0)[:, None, None] > 0.5
    old_moment = slot_moment[0]
    moment_slots = jnp.where(used, momentum_decay * old_moment + slot_update, old_moment)
    weight_slots = (slot_weights[0].astype(jnp.float32) - step_rate * moment_slots).astype(
        jnp.bfloat16
    )
    every_slot = lax.all_gather(weight_slots[None], ("dp", "group"), axis=0, tiled=True)
    chosen = every_slot[owners, slot_of]
    new_weights = chosen.reshape(2, piece_count * piece_rows // 2, features)
    return (new_errors, moment_slots[None], new_weights, new_norm_weights, new_norm_moment)


def solution(mesh):
    placed = (
        P(("dp", "group"), None, None, None),
        P(("dp", "group"), None, None, None),
        P(),
        P(("dp", "group"), None, None),
        P(),
        P(),
        P(),
        P(("dp", "group"), None, None, None),
        P(("dp", "group"), None, None, None),
    )
    return jax.shard_map(
        on_device,
        mesh=mesh,
        in_specs=placed,
        out_specs=(
            P(("dp", "group"), None, None, None),
            P(("dp", "group"), None, None, None),
            P(),
            P(),
            P(),
        ),
        check_vma=False,
    )
```

```python
import jax
import jax.numpy as jnp
from jax import lax
from jax.sharding import PartitionSpec as P

momentum_decay = 0.9
step_rate = 0.5
HI = lax.Precision.HIGHEST


def radix4_rounds(dp_size, group_size):
    z_size = 4
    y_size = dp_size // (2 * z_size)

    def dp_of(y, z, c):
        return (y * z_size + z) * 2 + c

    rounds = [[("dp", [(i, i ^ 1) for i in range(dp_size)])]]
    rounds.append([("group", [(i, i ^ s) for i in range(group_size)]) for s in (1, 2, 3)])
    for along_z in (True, False):
        parts = []
        for s in (1, 2, 3):
            perm = []
            for y in range(y_size):
                for z in range(z_size):
                    for c in range(2):
                        dst = dp_of(y, z ^ s, c) if along_z else dp_of(y ^ s, z, c)
                        perm.append((dp_of(y, z, c), dst))
            parts.append(("dp", perm))
        rounds.append(parts)
    return rounds


def sum_radix4(x, rounds):
    for parts in rounds:
        if len(parts) == 1:
            x = x + lax.ppermute(x, parts[0][0], parts[0][1])
        else:
            r1, r2, r3 = [lax.ppermute(x, axis, perm) for axis, perm in parts]
            x = (x + r1) + (r2 + r3)
    return x


def sum_all_to_all(x, count):
    axes = ("dp", "group")
    rows = lax.all_to_all(x.reshape(count, -1), axes, 0, 0, tiled=False)
    mine = jnp.sum(rows, axis=0)
    spread = jnp.broadcast_to(mine[None], (count,) + mine.shape)
    return lax.all_to_all(spread, axes, 0, 0, tiled=False).reshape(-1)


def orth_t(ft):
    gram = jnp.einsum("mrd,msd->mrs", ft, ft, precision=HI)
    lower_factor = jnp.linalg.cholesky(gram)
    return jax.scipy.linalg.solve_triangular(lower_factor, ft, lower=True)


def left_t(merged, right_t):
    return jnp.einsum("mdk,mrk->mrd", merged, right_t, precision=HI)


def right_t_of(merged, left_tr):
    return jnp.einsum("mdk,mrd->mrk", merged, left_tr, precision=HI)


def on_device(
    gradients,
    errors,
    warm_right,
    norm_grads,
    norm_weights,
    norm_moment,
    owners,
    slot_weights,
    slot_moment,
):
    dp_size = lax.axis_size("dp")
    group_size = lax.axis_size("group")
    replicas = dp_size * group_size
    rounds = radix4_rounds(dp_size, group_size)

    old_moment = slot_moment[0]
    carried = slot_weights[0].astype(jnp.float32) - (step_rate * momentum_decay) * old_moment
    every_carried = lax.all_gather(carried[None], ("dp", "group"), axis=0, tiled=True)

    merged = gradients[0].astype(jnp.float32) + errors[0]
    lshape = (merged.shape[0], warm_right.shape[2], merged.shape[1])
    p1 = left_t(merged, jnp.swapaxes(warm_right, 1, 2))
    norm_local = norm_grads[0]
    joined = jnp.concatenate([p1.reshape(-1), norm_local.reshape(-1)])
    joined_sum = sum_all_to_all(joined, replicas)
    p1_sum = joined_sum[: p1.size].reshape(lshape)
    norm_sum = joined_sum[p1.size :].reshape(norm_local.shape)
    left_one = orth_t(p1_sum)
    right_one = sum_radix4(right_t_of(merged, left_one), rounds) / replicas
    p2_sum = sum_all_to_all(left_t(merged, right_one).reshape(-1), replicas)
    left_two = orth_t(p2_sum.reshape(lshape))
    right_two = sum_radix4(right_t_of(merged, left_two), rounds) / replicas
    update = jnp.einsum("mrd,mrk->mdk", left_two, right_two, precision=HI)
    new_errors = (merged - update)[None]
    new_norm_moment = momentum_decay * norm_moment + norm_sum / replicas
    new_norm_weights = norm_weights - step_rate * new_norm_moment
    piece_count = owners.shape[0]
    slot_count = slot_moment.shape[1]
    piece_rows = slot_moment.shape[2]
    features = slot_moment.shape[3]
    positions = jnp.arange(piece_count, dtype=jnp.int32)
    same_owner = owners[:, None] == owners[None, :]
    earlier = positions[:, None] < positions[None, :]
    slot_of = jnp.sum((same_owner & earlier).astype(jnp.int32), axis=0)
    my_index = lax.axis_index(("dp", "group"))
    owned = owners == my_index
    slot_range = jnp.arange(slot_count, dtype=jnp.int32)
    selector = (owned[:, None] & (slot_of[:, None] == slot_range[None, :])).astype(jnp.float32)
    pieces = update.reshape(piece_count, piece_rows, features)
    slot_update = jnp.einsum("js,jrk->srk", selector, pieces, precision=HI)
    used = jnp.sum(selector, axis=0)[:, None, None] > 0.5
    moment_slots = jnp.where(used, momentum_decay * old_moment + slot_update, old_moment)
    chosen = every_carried[owners, slot_of] - step_rate * pieces
    new_weights = chosen.astype(jnp.bfloat16).reshape(2, piece_count * piece_rows // 2, features)
    return (new_errors, moment_slots[None], new_weights, new_norm_weights, new_norm_moment)


def solution(mesh):
    placed = (
        P(("dp", "group"), None, None, None),
        P(("dp", "group"), None, None, None),
        P(),
        P(("dp", "group"), None, None),
        P(),
        P(),
        P(),
        P(("dp", "group"), None, None, None),
        P(("dp", "group"), None, None, None),
    )
    return jax.shard_map(
        on_device,
        mesh=mesh,
        in_specs=placed,
        out_specs=(
            P(("dp", "group"), None, None, None),
            P(("dp", "group"), None, None, None),
            P(),
            P(),
            P(),
        ),
        check_vma=False,
    )
```

```python
import jax
import jax.numpy as jnp
from jax import lax
from jax.sharding import PartitionSpec as P

momentum_decay = 0.9
step_rate = 0.5
HI = lax.Precision.HIGHEST
MID = lax.Precision.HIGH


def radix4_rounds(dp_size, group_size):
    z_size = 4
    y_size = dp_size // (2 * z_size)

    def dp_of(y, z, c):
        return (y * z_size + z) * 2 + c

    rounds = [[("dp", [(i, i ^ 1) for i in range(dp_size)])]]
    rounds.append([("group", [(i, i ^ s) for i in range(group_size)]) for s in (1, 2, 3)])
    for along_z in (True, False):
        parts = []
        for s in (1, 2, 3):
            perm = []
            for y in range(y_size):
                for z in range(z_size):
                    for c in range(2):
                        dst = dp_of(y, z ^ s, c) if along_z else dp_of(y ^ s, z, c)
                        perm.append((dp_of(y, z, c), dst))
            parts.append(("dp", perm))
        rounds.append(parts)
    return rounds


def sum_radix4(x, rounds):
    for parts in rounds:
        if len(parts) == 1:
            x = x + lax.ppermute(x, parts[0][0], parts[0][1])
        else:
            r1, r2, r3 = [lax.ppermute(x, axis, perm) for axis, perm in parts]
            x = (x + r1) + (r2 + r3)
    return x


def sum_all_to_all(x, count):
    axes = ("dp", "group")
    rows = lax.all_to_all(x.reshape(count, -1), axes, 0, 0, tiled=False)
    mine = jnp.sum(rows, axis=0)
    spread = jnp.broadcast_to(mine[None], (count,) + mine.shape)
    return lax.all_to_all(spread, axes, 0, 0, tiled=False).reshape(-1)


def orth_t(ft):
    gram = jnp.einsum("mrd,msd->mrs", ft, ft, precision=HI)
    lower_factor = jnp.linalg.cholesky(gram)
    return jax.scipy.linalg.solve_triangular(lower_factor, ft, lower=True)


def left_t(merged, right_t):
    return jnp.einsum("mdk,mrk->mrd", merged, right_t, precision=MID)


def right_t_of(merged, left_tr):
    return jnp.einsum("mdk,mrd->mrk", merged, left_tr, precision=MID)


def on_device(
    gradients,
    errors,
    warm_right,
    norm_grads,
    norm_weights,
    norm_moment,
    owners,
    slot_weights,
    slot_moment,
):
    dp_size = lax.axis_size("dp")
    group_size = lax.axis_size("group")
    replicas = dp_size * group_size
    rounds = radix4_rounds(dp_size, group_size)

    old_moment = slot_moment[0]
    carried = slot_weights[0].astype(jnp.float32) - (step_rate * momentum_decay) * old_moment
    every_carried = lax.all_gather(carried[None], ("dp", "group"), axis=0, tiled=True)

    merged = gradients[0].astype(jnp.float32) + errors[0]
    lshape = (merged.shape[0], warm_right.shape[2], merged.shape[1])
    p1 = left_t(merged, jnp.swapaxes(warm_right, 1, 2))
    norm_local = norm_grads[0]
    joined = jnp.concatenate([p1.reshape(-1), norm_local.reshape(-1)])
    joined_sum = sum_all_to_all(joined, replicas)
    p1_sum = joined_sum[: p1.size].reshape(lshape)
    norm_sum = joined_sum[p1.size :].reshape(norm_local.shape)
    left_one = orth_t(p1_sum)
    right_one = sum_radix4(right_t_of(merged, left_one), rounds) / replicas
    p2_sum = sum_all_to_all(left_t(merged, right_one).reshape(-1), replicas)
    left_two = orth_t(p2_sum.reshape(lshape))
    right_two = sum_radix4(right_t_of(merged, left_two), rounds) / replicas
    update = jnp.einsum("mrd,mrk->mdk", left_two, right_two, precision=MID)
    new_errors = (merged - update)[None]
    new_norm_moment = momentum_decay * norm_moment + norm_sum / replicas
    new_norm_weights = norm_weights - step_rate * new_norm_moment
    piece_count = owners.shape[0]
    slot_count = slot_moment.shape[1]
    piece_rows = slot_moment.shape[2]
    features = slot_moment.shape[3]
    positions = jnp.arange(piece_count, dtype=jnp.int32)
    same_owner = owners[:, None] == owners[None, :]
    earlier = positions[:, None] < positions[None, :]
    slot_of = jnp.sum((same_owner & earlier).astype(jnp.int32), axis=0)
    my_index = lax.axis_index(("dp", "group"))
    owned = owners == my_index
    pieces_per_matrix = piece_count // merged.shape[0]
    moment_list = []
    for s in range(slot_count):
        hit = owned & (slot_of == s)
        piece = jnp.sum(jnp.where(hit, positions, 0))
        matrix = piece // pieces_per_matrix
        row0 = (piece % pieces_per_matrix) * piece_rows
        rows_l = lax.dynamic_slice(left_two, (matrix, 0, row0), (1, left_two.shape[1], piece_rows))[0]
        rows_r = lax.dynamic_index_in_dim(right_two, matrix, 0, keepdims=False)
        piece_update = jnp.einsum("rd,rk->dk", rows_l, rows_r, precision=MID)
        fresh = momentum_decay * old_moment[s] + piece_update
        moment_list.append(jnp.where(jnp.any(hit), fresh, old_moment[s]))
    moment_slots = jnp.stack(moment_list)
    pieces = update.reshape(piece_count, piece_rows, features)
    chosen = every_carried[owners, slot_of] - step_rate * pieces
    new_weights = chosen.astype(jnp.bfloat16).reshape(2, piece_count * piece_rows // 2, features)
    return (new_errors, moment_slots[None], new_weights, new_norm_weights, new_norm_moment)


def solution(mesh):
    placed = (
        P(("dp", "group"), None, None, None),
        P(("dp", "group"), None, None, None),
        P(),
        P(("dp", "group"), None, None),
        P(),
        P(),
        P(),
        P(("dp", "group"), None, None, None),
        P(("dp", "group"), None, None, None),
    )
    return jax.shard_map(
        on_device,
        mesh=mesh,
        in_specs=placed,
        out_specs=(
            P(("dp", "group"), None, None, None),
            P(("dp", "group"), None, None, None),
            P(),
            P(),
            P(),
        ),
        check_vma=False,
    )
```

```python
import jax
import jax.numpy as jnp
from jax import lax
from jax.sharding import PartitionSpec as P

momentum_decay = 0.9
step_rate = 0.5
HI = lax.Precision.HIGHEST
MID = lax.Precision.HIGH


def radix4_rounds(dp_size, group_size):
    z_size = 4
    y_size = dp_size // (2 * z_size)

    def dp_of(y, z, c):
        return (y * z_size + z) * 2 + c

    rounds = [[("dp", [(i, i ^ 1) for i in range(dp_size)])]]
    rounds.append([("group", [(i, i ^ s) for i in range(group_size)]) for s in (1, 2, 3)])
    for along_z in (True, False):
        parts = []
        for s in (1, 2, 3):
            perm = []
            for y in range(y_size):
                for z in range(z_size):
                    for c in range(2):
                        dst = dp_of(y, z ^ s, c) if along_z else dp_of(y ^ s, z, c)
                        perm.append((dp_of(y, z, c), dst))
            parts.append(("dp", perm))
        rounds.append(parts)
    return rounds


def sum_radix4(x, rounds):
    for parts in rounds:
        if len(parts) == 1:
            x = x + lax.ppermute(x, parts[0][0], parts[0][1])
        else:
            r1, r2, r3 = [lax.ppermute(x, axis, perm) for axis, perm in parts]
            x = (x + r1) + (r2 + r3)
    return x


def sum_all_to_all(x, count):
    axes = ("dp", "group")
    rows = lax.all_to_all(x.reshape(count, -1), axes, 0, 0, tiled=False)
    mine = jnp.sum(rows, axis=0)
    spread = jnp.broadcast_to(mine[None], (count,) + mine.shape)
    return lax.all_to_all(spread, axes, 0, 0, tiled=False).reshape(-1)


def gram_factor(ft):
    gram = jnp.einsum("mrd,msd->mrs", ft, ft, precision=HI)
    return jnp.linalg.cholesky(gram)


def solve_lower(lower_factor, rows):
    return jax.scipy.linalg.solve_triangular(lower_factor, rows, lower=True)


def left_t(merged, right_t):
    return jnp.einsum("mdk,mrk->mrd", merged, right_t, precision=MID)


def right_t_of(merged, left_tr):
    return jnp.einsum("mdk,mrd->mrk", merged, left_tr, precision=MID)


def on_device(
    gradients,
    errors,
    warm_right,
    norm_grads,
    norm_weights,
    norm_moment,
    owners,
    slot_weights,
    slot_moment,
):
    dp_size = lax.axis_size("dp")
    group_size = lax.axis_size("group")
    replicas = dp_size * group_size
    rounds = radix4_rounds(dp_size, group_size)

    old_moment = slot_moment[0]
    carried = slot_weights[0].astype(jnp.float32) - (step_rate * momentum_decay) * old_moment
    every_carried = lax.all_gather(carried[None], ("dp", "group"), axis=0, tiled=True)

    merged = gradients[0].astype(jnp.float32) + errors[0]
    lshape = (merged.shape[0], warm_right.shape[2], merged.shape[1])
    p1 = left_t(merged, jnp.swapaxes(warm_right, 1, 2))
    norm_local = norm_grads[0]
    joined = jnp.concatenate([p1.reshape(-1), norm_local.reshape(-1)])
    joined_sum = sum_all_to_all(joined, replicas)
    p1_sum = joined_sum[: p1.size].reshape(lshape)
    norm_sum = joined_sum[p1.size :].reshape(norm_local.shape)
    lower_one = gram_factor(p1_sum)
    q1_sum = sum_radix4(right_t_of(merged, p1_sum), rounds)
    right_one = solve_lower(lower_one, q1_sum) / replicas
    p2_sum = sum_all_to_all(left_t(merged, right_one).reshape(-1), replicas).reshape(lshape)
    lower_two = gram_factor(p2_sum)
    left_two = solve_lower(lower_two, p2_sum)
    q2_sum = sum_radix4(right_t_of(merged, p2_sum), rounds)
    right_two = solve_lower(lower_two, q2_sum) / replicas
    update = jnp.einsum("mrd,mrk->mdk", left_two, right_two, precision=MID)
    new_errors = (merged - update)[None]
    new_norm_moment = momentum_decay * norm_moment + norm_sum / replicas
    new_norm_weights = norm_weights - step_rate * new_norm_moment
    piece_count = owners.shape[0]
    slot_count = slot_moment.shape[1]
    piece_rows = slot_moment.shape[2]
    features = slot_moment.shape[3]
    positions = jnp.arange(piece_count, dtype=jnp.int32)
    same_owner = owners[:, None] == owners[None, :]
    earlier = positions[:, None] < positions[None, :]
    slot_of = jnp.sum((same_owner & earlier).astype(jnp.int32), axis=0)
    my_index = lax.axis_index(("dp", "group"))
    owned = owners == my_index
    pieces_per_matrix = piece_count // merged.shape[0]
    moment_list = []
    for s in range(slot_count):
        hit = owned & (slot_of == s)
        piece = jnp.sum(jnp.where(hit, positions, 0))
        matrix = piece // pieces_per_matrix
        row0 = (piece % pieces_per_matrix) * piece_rows
        rows_l = lax.dynamic_slice(left_two, (matrix, 0, row0), (1, left_two.shape[1], piece_rows))[0]
        rows_r = lax.dynamic_index_in_dim(right_two, matrix, 0, keepdims=False)
        piece_update = jnp.einsum("rd,rk->dk", rows_l, rows_r, precision=MID)
        fresh = momentum_decay * old_moment[s] + piece_update
        moment_list.append(jnp.where(jnp.any(hit), fresh, old_moment[s]))
    moment_slots = jnp.stack(moment_list)
    pieces = update.reshape(piece_count, piece_rows, features)
    chosen = every_carried[owners, slot_of] - step_rate * pieces
    new_weights = chosen.astype(jnp.bfloat16).reshape(2, piece_count * piece_rows // 2, features)
    return (new_errors, moment_slots[None], new_weights, new_norm_weights, new_norm_moment)


def solution(mesh):
    placed = (
        P(("dp", "group"), None, None, None),
        P(("dp", "group"), None, None, None),
        P(),
        P(("dp", "group"), None, None),
        P(),
        P(),
        P(),
        P(("dp", "group"), None, None, None),
        P(("dp", "group"), None, None, None),
    )
    return jax.shard_map(
        on_device,
        mesh=mesh,
        in_specs=placed,
        out_specs=(
            P(("dp", "group"), None, None, None),
            P(("dp", "group"), None, None, None),
            P(),
            P(),
            P(),
        ),
        check_vma=False,
    )
```

```python
import jax
import jax.numpy as jnp
from jax import lax
from jax.experimental import pallas as pl
from jax.experimental.pallas import tpu as pltpu
from jax.sharding import PartitionSpec as P

momentum_decay = 0.9
step_rate = 0.5
HI = lax.Precision.HIGHEST
MID = lax.Precision.HIGH


def radix4_rounds(dp_size, group_size):
    z_size = 4
    y_size = dp_size // (2 * z_size)

    def dp_of(y, z, c):
        return (y * z_size + z) * 2 + c

    rounds = [[("dp", [(i, i ^ 1) for i in range(dp_size)])]]
    rounds.append([("group", [(i, i ^ s) for i in range(group_size)]) for s in (1, 2, 3)])
    for along_z in (True, False):
        parts = []
        for s in (1, 2, 3):
            perm = []
            for y in range(y_size):
                for z in range(z_size):
                    for c in range(2):
                        dst = dp_of(y, z ^ s, c) if along_z else dp_of(y ^ s, z, c)
                        perm.append((dp_of(y, z, c), dst))
            parts.append(("dp", perm))
        rounds.append(parts)
    return rounds


def sum_radix4(x, rounds):
    for parts in rounds:
        if len(parts) == 1:
            x = x + lax.ppermute(x, parts[0][0], parts[0][1])
        else:
            r1, r2, r3 = [lax.ppermute(x, axis, perm) for axis, perm in parts]
            x = (x + r1) + (r2 + r3)
    return x


def sum_all_to_all(x, count):
    axes = ("dp", "group")
    rows = lax.all_to_all(x.reshape(count, -1), axes, 0, 0, tiled=False)
    mine = jnp.sum(rows, axis=0)
    spread = jnp.broadcast_to(mine[None], (count,) + mine.shape)
    return lax.all_to_all(spread, axes, 0, 0, tiled=False).reshape(-1)


def gram_factor(ft):
    gram = jnp.einsum("mrd,msd->mrs", ft, ft, precision=HI)
    return jnp.linalg.cholesky(gram)


def solve_lower(lower_factor, rows):
    return jax.scipy.linalg.solve_triangular(lower_factor, rows, lower=True)


def left_t(merged, right_t):
    return jnp.einsum("mdk,mrk->mrd", merged, right_t, precision=MID)


def right_t_of(merged, left_tr):
    return jnp.einsum("mdk,mrd->mrk", merged, left_tr, precision=MID)


TAIL_ROWS = 256


def tail_kernel(table, grads, errs, left_rows, right_t, carried, out_err, out_w, cbuf, sems):
    m = pl.program_id(0)
    i = pl.program_id(1)
    per_block = cbuf.shape[0]
    piece_rows = cbuf.shape[1]
    blocks = pl.num_programs(1)
    base = (m * blocks + i) * per_block
    copies = []
    for p in range(per_block):
        cp = pltpu.make_async_copy(carried.at[table[base + p]], cbuf.at[p], sems.at[p])
        cp.start()
        copies.append(cp)
    upd = jnp.dot(left_rows[0], right_t[0], precision=HI, preferred_element_type=jnp.float32)
    merged = grads[0].astype(jnp.float32) + errs[0]
    out_err[0] = merged - upd
    for p in range(per_block):
        copies[p].wait()
        rows = slice(p * piece_rows, (p + 1) * piece_rows)
        out_w[0, rows, :] = (cbuf[p] - step_rate * upd[rows, :]).astype(out_w.dtype)


def tail(table, grads, errs, left_rows, right_t, carried):
    mats, dw, kv = grads.shape
    rank = left_rows.shape[2]
    piece_rows = carried.shape[1]
    per_block = TAIL_ROWS // piece_rows
    grid = (mats, dw // TAIL_ROWS)
    row_spec = pl.BlockSpec((1, TAIL_ROWS, kv), lambda m, i, t: (m, i, 0))
    spec = pltpu.PrefetchScalarGridSpec(
        num_scalar_prefetch=1,
        grid=grid,
        in_specs=[
            row_spec,
            row_spec,
            pl.BlockSpec((1, TAIL_ROWS, rank), lambda m, i, t: (m, i, 0)),
            pl.BlockSpec((1, rank, kv), lambda m, i, t: (m, 0, 0)),
            pl.BlockSpec(memory_space=pl.ANY),
        ],
        out_specs=[row_spec, row_spec],
        scratch_shapes=[
            pltpu.VMEM((per_block, piece_rows, kv), jnp.float32),
            pltpu.SemaphoreType.DMA((per_block,)),
        ],
    )
    elems = mats * dw * kv
    cost = pl.CostEstimate(flops=2 * elems * rank, transcendentals=0, bytes_accessed=elems * (2 + 4 + 4 + 4 + 2))
    return pl.pallas_call(
        tail_kernel,
        grid_spec=spec,
        out_shape=[
            jax.ShapeDtypeStruct((mats, dw, kv), jnp.float32),
            jax.ShapeDtypeStruct((mats, dw, kv), jnp.bfloat16),
        ],
        cost_estimate=cost,
    )(table, grads, errs, left_rows, right_t, carried)


def on_device(
    gradients,
    errors,
    warm_right,
    norm_grads,
    norm_weights,
    norm_moment,
    owners,
    slot_weights,
    slot_moment,
):
    dp_size = lax.axis_size("dp")
    group_size = lax.axis_size("group")
    replicas = dp_size * group_size
    rounds = radix4_rounds(dp_size, group_size)

    old_moment = slot_moment[0]
    carried = slot_weights[0].astype(jnp.float32) - (step_rate * momentum_decay) * old_moment
    every_carried = lax.all_gather(carried[None], ("dp", "group"), axis=0, tiled=True)

    merged = gradients[0].astype(jnp.float32) + errors[0]
    lshape = (merged.shape[0], warm_right.shape[2], merged.shape[1])
    p1 = left_t(merged, jnp.swapaxes(warm_right, 1, 2))
    norm_local = norm_grads[0]
    joined = jnp.concatenate([p1.reshape(-1), norm_local.reshape(-1)])
    joined_sum = sum_all_to_all(joined, replicas)
    p1_sum = joined_sum[: p1.size].reshape(lshape)
    norm_sum = joined_sum[p1.size :].reshape(norm_local.shape)
    lower_one = gram_factor(p1_sum)
    q1_sum = sum_radix4(right_t_of(merged, p1_sum), rounds)
    right_one = solve_lower(lower_one, q1_sum) / replicas
    p2_sum = sum_all_to_all(left_t(merged, right_one).reshape(-1), replicas).reshape(lshape)
    lower_two = gram_factor(p2_sum)
    left_two = solve_lower(lower_two, p2_sum)
    q2_sum = sum_radix4(right_t_of(merged, p2_sum), rounds)
    right_two = solve_lower(lower_two, q2_sum) / replicas
    new_norm_moment = momentum_decay * norm_moment + norm_sum / replicas
    new_norm_weights = norm_weights - step_rate * new_norm_moment
    piece_count = owners.shape[0]
    slot_count = slot_moment.shape[1]
    piece_rows = slot_moment.shape[2]
    features = slot_moment.shape[3]
    positions = jnp.arange(piece_count, dtype=jnp.int32)
    same_owner = owners[:, None] == owners[None, :]
    earlier = positions[:, None] < positions[None, :]
    slot_of = jnp.sum((same_owner & earlier).astype(jnp.int32), axis=0)
    my_index = lax.axis_index(("dp", "group"))
    owned = owners == my_index
    pieces_per_matrix = piece_count // merged.shape[0]
    moment_list = []
    for s in range(slot_count):
        hit = owned & (slot_of == s)
        piece = jnp.sum(jnp.where(hit, positions, 0))
        matrix = piece // pieces_per_matrix
        row0 = (piece % pieces_per_matrix) * piece_rows
        rows_l = lax.dynamic_slice(left_two, (matrix, 0, row0), (1, left_two.shape[1], piece_rows))[0]
        rows_r = lax.dynamic_index_in_dim(right_two, matrix, 0, keepdims=False)
        piece_update = jnp.einsum("rd,rk->dk", rows_l, rows_r, precision=MID)
        fresh = momentum_decay * old_moment[s] + piece_update
        moment_list.append(jnp.where(jnp.any(hit), fresh, old_moment[s]))
    moment_slots = jnp.stack(moment_list)
    table = jnp.clip(owners * slot_count + slot_of, 0, every_carried.shape[0] * slot_count - 1)
    carried_rows = every_carried.reshape(-1, piece_rows, features)
    new_errors, new_weights = tail(
        table, gradients[0], errors[0], jnp.swapaxes(left_two, 1, 2), right_two, carried_rows
    )
    new_errors = new_errors[None]
    return (new_errors, moment_slots[None], new_weights, new_norm_weights, new_norm_moment)


def solution(mesh):
    placed = (
        P(("dp", "group"), None, None, None),
        P(("dp", "group"), None, None, None),
        P(),
        P(("dp", "group"), None, None),
        P(),
        P(),
        P(),
        P(("dp", "group"), None, None, None),
        P(("dp", "group"), None, None, None),
    )
    return jax.shard_map(
        on_device,
        mesh=mesh,
        in_specs=placed,
        out_specs=(
            P(("dp", "group"), None, None, None),
            P(("dp", "group"), None, None, None),
            P(),
            P(),
            P(),
        ),
        check_vma=False,
    )
```

```python
import jax
import jax.numpy as jnp
from jax import lax
from jax.experimental import pallas as pl
from jax.experimental.pallas import tpu as pltpu
from jax.sharding import PartitionSpec as P

momentum_decay = 0.9
step_rate = 0.5
HI = lax.Precision.HIGHEST
MID = lax.Precision.HIGH


def radix4_rounds(dp_size, group_size):
    z_size = 4
    y_size = dp_size // (2 * z_size)

    def dp_of(y, z, c):
        return (y * z_size + z) * 2 + c

    rounds = [[("dp", [(i, i ^ 1) for i in range(dp_size)])]]
    rounds.append([("group", [(i, i ^ s) for i in range(group_size)]) for s in (1, 2, 3)])
    for along_z in (True, False):
        parts = []
        for s in (1, 2, 3):
            perm = []
            for y in range(y_size):
                for z in range(z_size):
                    for c in range(2):
                        dst = dp_of(y, z ^ s, c) if along_z else dp_of(y ^ s, z, c)
                        perm.append((dp_of(y, z, c), dst))
            parts.append(("dp", perm))
        rounds.append(parts)
    return rounds


def sum_radix4(x, rounds):
    for parts in rounds:
        if len(parts) == 1:
            x = x + lax.ppermute(x, parts[0][0], parts[0][1])
        else:
            r1, r2, r3 = [lax.ppermute(x, axis, perm) for axis, perm in parts]
            x = (x + r1) + (r2 + r3)
    return x


def sum_all_to_all(x, count):
    axes = ("dp", "group")
    rows = lax.all_to_all(x.reshape(count, -1), axes, 0, 0, tiled=False)
    mine = jnp.sum(rows, axis=0)
    spread = jnp.broadcast_to(mine[None], (count,) + mine.shape)
    return lax.all_to_all(spread, axes, 0, 0, tiled=False).reshape(-1)


def gram_factor(ft):
    gram = jnp.einsum("mrd,msd->mrs", ft, ft, precision=HI)
    return jnp.linalg.cholesky(gram)


def solve_lower(lower_factor, rows):
    return jax.scipy.linalg.solve_triangular(lower_factor, rows, lower=True)


def left_t(merged, right_t):
    return jnp.einsum("mdk,mrk->mrd", merged, right_t, precision=MID)


def right_t_of(merged, left_tr):
    return jnp.einsum("mdk,mrd->mrk", merged, left_tr, precision=MID)


TAIL_ROWS = 512


def tail_kernel(table, grads, errs, left_rows, right_t, carried, out_err, out_w, cbuf, sems):
    m = pl.program_id(0)
    i = pl.program_id(1)
    pieces = cbuf.shape[0]
    piece_rows = cbuf.shape[1]
    blocks = pl.num_programs(1)
    per_block = out_w.shape[1] // piece_rows

    def piece_copy(j):
        return pltpu.make_async_copy(carried.at[table[j]], cbuf.at[j], sems.at[j])

    @pl.when((m == 0) & (i == 0))
    def _():
        for j in range(pieces):
            piece_copy(j).start()

    upd = jnp.dot(left_rows[0], right_t[0], precision=HI, preferred_element_type=jnp.float32)
    merged = grads[0].astype(jnp.float32) + errs[0]
    out_err[0] = merged - upd
    base = (m * blocks + i) * per_block
    for p in range(per_block):
        piece_copy(base + p).wait()
    for p in range(per_block):
        rows = slice(p * piece_rows, (p + 1) * piece_rows)
        out_w[0, rows, :] = (cbuf[base + p] - step_rate * upd[rows, :]).astype(out_w.dtype)


def tail(table, grads, errs, left_rows, right_t, carried):
    mats, dw, kv = grads.shape
    rank = left_rows.shape[2]
    piece_rows = carried.shape[1]
    pieces = mats * dw // piece_rows
    grid = (mats, dw // TAIL_ROWS)
    row_spec = pl.BlockSpec((1, TAIL_ROWS, kv), lambda m, i, t: (m, i, 0))
    spec = pltpu.PrefetchScalarGridSpec(
        num_scalar_prefetch=1,
        grid=grid,
        in_specs=[
            row_spec,
            row_spec,
            pl.BlockSpec((1, TAIL_ROWS, rank), lambda m, i, t: (m, i, 0)),
            pl.BlockSpec((1, rank, kv), lambda m, i, t: (m, 0, 0)),
            pl.BlockSpec(memory_space=pl.ANY),
        ],
        out_specs=[row_spec, row_spec],
        scratch_shapes=[
            pltpu.VMEM((pieces, piece_rows, kv), jnp.float32),
            pltpu.SemaphoreType.DMA((pieces,)),
        ],
    )
    elems = mats * dw * kv
    cost = pl.CostEstimate(flops=2 * elems * rank, transcendentals=0, bytes_accessed=elems * (2 + 4 + 4 + 4 + 2))
    return pl.pallas_call(
        tail_kernel,
        grid_spec=spec,
        out_shape=[
            jax.ShapeDtypeStruct((mats, dw, kv), jnp.float32),
            jax.ShapeDtypeStruct((mats, dw, kv), jnp.bfloat16),
        ],
        cost_estimate=cost,
        compiler_params=pltpu.CompilerParams(
            dimension_semantics=("arbitrary", "arbitrary"), vmem_limit_bytes=48 * 1024 * 1024
        ),
    )(table, grads, errs, left_rows, right_t, carried)


def on_device(
    gradients,
    errors,
    warm_right,
    norm_grads,
    norm_weights,
    norm_moment,
    owners,
    slot_weights,
    slot_moment,
):
    dp_size = lax.axis_size("dp")
    group_size = lax.axis_size("group")
    replicas = dp_size * group_size
    rounds = radix4_rounds(dp_size, group_size)

    old_moment = slot_moment[0]
    carried = slot_weights[0].astype(jnp.float32) - (step_rate * momentum_decay) * old_moment
    every_carried = lax.all_gather(carried[None], ("dp", "group"), axis=0, tiled=True)

    merged = gradients[0].astype(jnp.float32) + errors[0]
    lshape = (merged.shape[0], warm_right.shape[2], merged.shape[1])
    p1 = left_t(merged, jnp.swapaxes(warm_right, 1, 2))
    norm_local = norm_grads[0]
    joined = jnp.concatenate([p1.reshape(-1), norm_local.reshape(-1)])
    joined_sum = sum_all_to_all(joined, replicas)
    p1_sum = joined_sum[: p1.size].reshape(lshape)
    norm_sum = joined_sum[p1.size :].reshape(norm_local.shape)
    lower_one = gram_factor(p1_sum)
    q1_sum = sum_radix4(right_t_of(merged, p1_sum), rounds)
    right_one = solve_lower(lower_one, q1_sum) / replicas
    p2_sum = sum_all_to_all(left_t(merged, right_one).reshape(-1), replicas).reshape(lshape)
    lower_two = gram_factor(p2_sum)
    left_two = solve_lower(lower_two, p2_sum)
    q2_sum = sum_radix4(right_t_of(merged, p2_sum), rounds)
    right_two = solve_lower(lower_two, q2_sum) / replicas
    new_norm_moment = momentum_decay * norm_moment + norm_sum / replicas
    new_norm_weights = norm_weights - step_rate * new_norm_moment
    piece_count = owners.shape[0]
    slot_count = slot_moment.shape[1]
    piece_rows = slot_moment.shape[2]
    features = slot_moment.shape[3]
    positions = jnp.arange(piece_count, dtype=jnp.int32)
    same_owner = owners[:, None] == owners[None, :]
    earlier = positions[:, None] < positions[None, :]
    slot_of = jnp.sum((same_owner & earlier).astype(jnp.int32), axis=0)
    my_index = lax.axis_index(("dp", "group"))
    owned = owners == my_index
    pieces_per_matrix = piece_count // merged.shape[0]
    moment_list = []
    for s in range(slot_count):
        hit = owned & (slot_of == s)
        piece = jnp.sum(jnp.where(hit, positions, 0))
        matrix = piece // pieces_per_matrix
        row0 = (piece % pieces_per_matrix) * piece_rows
        rows_l = lax.dynamic_slice(left_two, (matrix, 0, row0), (1, left_two.shape[1], piece_rows))[0]
        rows_r = lax.dynamic_index_in_dim(right_two, matrix, 0, keepdims=False)
        piece_update = jnp.einsum("rd,rk->dk", rows_l, rows_r, precision=MID)
        fresh = momentum_decay * old_moment[s] + piece_update
        moment_list.append(jnp.where(jnp.any(hit), fresh, old_moment[s]))
    moment_slots = jnp.stack(moment_list)
    table = jnp.clip(owners * slot_count + slot_of, 0, every_carried.shape[0] * slot_count - 1)
    carried_rows = every_carried.reshape(-1, piece_rows, features)
    new_errors, new_weights = tail(
        table, gradients[0], errors[0], jnp.swapaxes(left_two, 1, 2), right_two, carried_rows
    )
    new_errors = new_errors[None]
    return (new_errors, moment_slots[None], new_weights, new_norm_weights, new_norm_moment)


def solution(mesh):
    placed = (
        P(("dp", "group"), None, None, None),
        P(("dp", "group"), None, None, None),
        P(),
        P(("dp", "group"), None, None),
        P(),
        P(),
        P(),
        P(("dp", "group"), None, None, None),
        P(("dp", "group"), None, None, None),
    )
    return jax.shard_map(
        on_device,
        mesh=mesh,
        in_specs=placed,
        out_specs=(
            P(("dp", "group"), None, None, None),
            P(("dp", "group"), None, None, None),
            P(),
            P(),
            P(),
        ),
        check_vma=False,
    )
```

```python
import jax
import jax.numpy as jnp
from jax import lax
from jax.experimental import pallas as pl
from jax.experimental.pallas import tpu as pltpu
from jax.sharding import PartitionSpec as P

momentum_decay = 0.9
step_rate = 0.5
HI = lax.Precision.HIGHEST
MID = lax.Precision.HIGH


def radix4_rounds(dp_size, group_size):
    z_size = 4
    y_size = dp_size // (2 * z_size)

    def dp_of(y, z, c):
        return (y * z_size + z) * 2 + c

    rounds = [[("dp", [(i, i ^ 1) for i in range(dp_size)])]]
    rounds.append([("group", [(i, i ^ s) for i in range(group_size)]) for s in (1, 2, 3)])
    for along_z in (True, False):
        parts = []
        for s in (1, 2, 3):
            perm = []
            for y in range(y_size):
                for z in range(z_size):
                    for c in range(2):
                        dst = dp_of(y, z ^ s, c) if along_z else dp_of(y ^ s, z, c)
                        perm.append((dp_of(y, z, c), dst))
            parts.append(("dp", perm))
        rounds.append(parts)
    return rounds


def sum_radix4(x, rounds):
    for parts in rounds:
        if len(parts) == 1:
            x = x + lax.ppermute(x, parts[0][0], parts[0][1])
        else:
            r1, r2, r3 = [lax.ppermute(x, axis, perm) for axis, perm in parts]
            x = (x + r1) + (r2 + r3)
    return x


def sum_all_to_all(x, count):
    axes = ("dp", "group")
    rows = lax.all_to_all(x.reshape(count, -1), axes, 0, 0, tiled=False)
    mine = jnp.sum(rows, axis=0)
    spread = jnp.broadcast_to(mine[None], (count,) + mine.shape)
    return lax.all_to_all(spread, axes, 0, 0, tiled=False).reshape(-1)


def gram_factor(ft):
    gram = jnp.einsum("mrd,msd->mrs", ft, ft, precision=HI)
    return jnp.linalg.cholesky(gram)


def solve_lower(lower_factor, rows):
    return jax.scipy.linalg.solve_triangular(lower_factor, rows, lower=True)


def left_t(merged, right_t):
    return jnp.einsum("mdk,mrk->mrd", merged, right_t, precision=MID)


def right_t_of(merged, left_tr):
    return jnp.einsum("mdk,mrd->mrk", merged, left_tr, precision=MID)


TAIL_ROWS = 512


def tail_kernel(table, grads, errs, left_rows, right_t, carried, out_err, out_w, cbuf, ubuf, sems):
    m = pl.program_id(0)
    i = pl.program_id(1)
    pieces = cbuf.shape[0]
    piece_rows = cbuf.shape[1]
    blocks = pl.num_programs(1)
    per_block = out_w.shape[1] // piece_rows

    def piece_copy(j):
        return pltpu.make_async_copy(carried.at[table[j]], cbuf.at[j], sems.at[j])

    @pl.when((m == 0) & (i == 0))
    def _():
        def start(j, carry):
            piece_copy(j).start()
            return carry

        lax.fori_loop(0, pieces, start, 0)

    upd = jnp.dot(left_rows[0], right_t[0], precision=HI, preferred_element_type=jnp.float32)
    merged = grads[0].astype(jnp.float32) + errs[0]
    out_err[0] = merged - upd
    ubuf[...] = upd
    base = (m * blocks + i) * per_block

    def finish(p, carry):
        piece_copy(base + p).wait()
        rows = pl.ds(pl.multiple_of(p * piece_rows, piece_rows), piece_rows)
        out_w[0, rows, :] = (cbuf[base + p] - step_rate * ubuf[rows, :]).astype(out_w.dtype)
        return carry

    lax.fori_loop(0, per_block, finish, 0)


def tail(table, grads, errs, left_rows, right_t, carried):
    mats, dw, kv = grads.shape
    rank = left_rows.shape[2]
    piece_rows = carried.shape[1]
    pieces = mats * dw // piece_rows
    grid = (mats, dw // TAIL_ROWS)
    row_spec = pl.BlockSpec((1, TAIL_ROWS, kv), lambda m, i, t: (m, i, 0))
    spec = pltpu.PrefetchScalarGridSpec(
        num_scalar_prefetch=1,
        grid=grid,
        in_specs=[
            row_spec,
            row_spec,
            pl.BlockSpec((1, TAIL_ROWS, rank), lambda m, i, t: (m, i, 0)),
            pl.BlockSpec((1, rank, kv), lambda m, i, t: (m, 0, 0)),
            pl.BlockSpec(memory_space=pl.ANY),
        ],
        out_specs=[row_spec, row_spec],
        scratch_shapes=[
            pltpu.VMEM((pieces, piece_rows, kv), jnp.float32),
            pltpu.VMEM((TAIL_ROWS, kv), jnp.float32),
            pltpu.SemaphoreType.DMA((pieces,)),
        ],
    )
    elems = mats * dw * kv
    cost = pl.CostEstimate(flops=2 * elems * rank, transcendentals=0, bytes_accessed=elems * (2 + 4 + 4 + 4 + 2))
    return pl.pallas_call(
        tail_kernel,
        grid_spec=spec,
        out_shape=[
            jax.ShapeDtypeStruct((mats, dw, kv), jnp.float32),
            jax.ShapeDtypeStruct((mats, dw, kv), jnp.bfloat16),
        ],
        cost_estimate=cost,
        compiler_params=pltpu.CompilerParams(
            dimension_semantics=("arbitrary", "arbitrary"), vmem_limit_bytes=48 * 1024 * 1024
        ),
    )(table, grads, errs, left_rows, right_t, carried)


def on_device(
    gradients,
    errors,
    warm_right,
    norm_grads,
    norm_weights,
    norm_moment,
    owners,
    slot_weights,
    slot_moment,
):
    dp_size = lax.axis_size("dp")
    group_size = lax.axis_size("group")
    replicas = dp_size * group_size
    rounds = radix4_rounds(dp_size, group_size)

    old_moment = slot_moment[0]
    carried = slot_weights[0].astype(jnp.float32) - (step_rate * momentum_decay) * old_moment

    merged = gradients[0].astype(jnp.float32) + errors[0]
    lshape = (merged.shape[0], warm_right.shape[2], merged.shape[1])
    p1 = left_t(merged, jnp.swapaxes(warm_right, 1, 2))
    norm_local = norm_grads[0]
    joined = jnp.concatenate([p1.reshape(-1), norm_local.reshape(-1)])
    joined_sum = sum_all_to_all(joined, replicas)
    joined_sum, carried = lax.optimization_barrier((joined_sum, carried))
    every_carried = lax.all_gather(carried[None], ("dp", "group"), axis=0, tiled=True)
    p1_sum = joined_sum[: p1.size].reshape(lshape)
    norm_sum = joined_sum[p1.size :].reshape(norm_local.shape)
    lower_one = gram_factor(p1_sum)
    q1_sum = sum_radix4(right_t_of(merged, p1_sum), rounds)
    right_one = solve_lower(lower_one, q1_sum) / replicas
    p2_sum = sum_all_to_all(left_t(merged, right_one).reshape(-1), replicas).reshape(lshape)
    lower_two = gram_factor(p2_sum)
    left_two = solve_lower(lower_two, p2_sum)
    q2_sum = sum_radix4(right_t_of(merged, p2_sum), rounds)
    right_two = solve_lower(lower_two, q2_sum) / replicas
    new_norm_moment = momentum_decay * norm_moment + norm_sum / replicas
    new_norm_weights = norm_weights - step_rate * new_norm_moment
    piece_count = owners.shape[0]
    slot_count = slot_moment.shape[1]
    piece_rows = slot_moment.shape[2]
    features = slot_moment.shape[3]
    positions = jnp.arange(piece_count, dtype=jnp.int32)
    same_owner = owners[:, None] == owners[None, :]
    earlier = positions[:, None] < positions[None, :]
    slot_of = jnp.sum((same_owner & earlier).astype(jnp.int32), axis=0)
    my_index = lax.axis_index(("dp", "group"))
    owned = owners == my_index
    pieces_per_matrix = piece_count // merged.shape[0]
    moment_list = []
    for s in range(slot_count):
        hit = owned & (slot_of == s)
        piece = jnp.sum(jnp.where(hit, positions, 0))
        matrix = piece // pieces_per_matrix
        row0 = (piece % pieces_per_matrix) * piece_rows
        rows_l = lax.dynamic_slice(left_two, (matrix, 0, row0), (1, left_two.shape[1], piece_rows))[0]
        rows_r = lax.dynamic_index_in_dim(right_two, matrix, 0, keepdims=False)
        piece_update = jnp.einsum("rd,rk->dk", rows_l, rows_r, precision=MID)
        fresh = momentum_decay * old_moment[s] + piece_update
        moment_list.append(jnp.where(jnp.any(hit), fresh, old_moment[s]))
    moment_slots = jnp.stack(moment_list)
    table = jnp.clip(owners * slot_count + slot_of, 0, every_carried.shape[0] * slot_count - 1)
    carried_rows = every_carried.reshape(-1, piece_rows, features)
    new_errors, new_weights = tail(
        table, gradients[0], errors[0], jnp.swapaxes(left_two, 1, 2), right_two, carried_rows
    )
    new_errors = new_errors[None]
    return (new_errors, moment_slots[None], new_weights, new_norm_weights, new_norm_moment)


def solution(mesh):
    placed = (
        P(("dp", "group"), None, None, None),
        P(("dp", "group"), None, None, None),
        P(),
        P(("dp", "group"), None, None),
        P(),
        P(),
        P(),
        P(("dp", "group"), None, None, None),
        P(("dp", "group"), None, None, None),
    )
    return jax.shard_map(
        on_device,
        mesh=mesh,
        in_specs=placed,
        out_specs=(
            P(("dp", "group"), None, None, None),
            P(("dp", "group"), None, None, None),
            P(),
            P(),
            P(),
        ),
        check_vma=False,
    )
```

```python
import jax
import jax.numpy as jnp
from jax import lax
from jax.experimental import pallas as pl
from jax.experimental.pallas import tpu as pltpu
from jax.sharding import PartitionSpec as P

momentum_decay = 0.9
step_rate = 0.5
HI = lax.Precision.HIGHEST
MID = lax.Precision.HIGH


def radix4_rounds(dp_size, group_size):
    z_size = 4
    y_size = dp_size // (2 * z_size)

    def dp_of(y, z, c):
        return (y * z_size + z) * 2 + c

    rounds = [[("dp", [(i, i ^ 1) for i in range(dp_size)])]]
    rounds.append([("group", [(i, i ^ s) for i in range(group_size)]) for s in (1, 2, 3)])
    for along_z in (True, False):
        parts = []
        for s in (1, 2, 3):
            perm = []
            for y in range(y_size):
                for z in range(z_size):
                    for c in range(2):
                        dst = dp_of(y, z ^ s, c) if along_z else dp_of(y ^ s, z, c)
                        perm.append((dp_of(y, z, c), dst))
            parts.append(("dp", perm))
        rounds.append(parts)
    return rounds


def sum_radix4(x, rounds):
    for parts in rounds:
        if len(parts) == 1:
            x = x + lax.ppermute(x, parts[0][0], parts[0][1])
        else:
            r1, r2, r3 = [lax.ppermute(x, axis, perm) for axis, perm in parts]
            x = (x + r1) + (r2 + r3)
    return x


def sum_all_to_all(x, count):
    axes = ("dp", "group")
    rows = lax.all_to_all(x.reshape(count, -1), axes, 0, 0, tiled=False)
    mine = jnp.sum(rows, axis=0)
    spread = jnp.broadcast_to(mine[None], (count,) + mine.shape)
    return lax.all_to_all(spread, axes, 0, 0, tiled=False).reshape(-1)


def gram_factor(ft):
    gram = jnp.einsum("mrd,msd->mrs", ft, ft, precision=HI)
    return jnp.linalg.cholesky(gram)


def solve_lower(lower_factor, rows):
    return jax.scipy.linalg.solve_triangular(lower_factor, rows, lower=True)


def left_t(merged, right_t):
    return jnp.einsum("mdk,mrk->mrd", merged, right_t, precision=MID)


def right_t_of(merged, left_tr):
    return jnp.einsum("mdk,mrd->mrk", merged, left_tr, precision=MID)


TAIL_ROWS = 512


def tail_kernel(table, grads, errs, left_rows, right_t, carried, out_err, out_w, cbuf, ubuf, sems):
    m = pl.program_id(0)
    i = pl.program_id(1)
    pieces = cbuf.shape[0]
    piece_rows = cbuf.shape[1]
    blocks = pl.num_programs(1)
    per_block = out_w.shape[1] // piece_rows

    def piece_copy(j):
        return pltpu.make_async_copy(carried.at[table[j]], cbuf.at[j], sems.at[j])

    @pl.when((m == 0) & (i == 0))
    def _():
        def start(j, carry):
            piece_copy(j).start()
            return carry

        lax.fori_loop(0, pieces, start, 0)

    upd = jnp.dot(left_rows[0], right_t[0], precision=HI, preferred_element_type=jnp.float32)
    merged = grads[0].astype(jnp.float32) + errs[0]
    out_err[0] = merged - upd
    ubuf[...] = upd
    base = (m * blocks + i) * per_block

    def finish(p, carry):
        piece_copy(base + p).wait()
        rows = pl.ds(pl.multiple_of(p * piece_rows, piece_rows), piece_rows)
        out_w[0, rows, :] = (cbuf[base + p] - step_rate * ubuf[rows, :]).astype(out_w.dtype)
        return carry

    lax.fori_loop(0, per_block, finish, 0)


def tail(table, grads, errs, left_rows, right_t, carried):
    mats, dw, kv = grads.shape
    rank = left_rows.shape[2]
    piece_rows = carried.shape[1]
    pieces = mats * dw // piece_rows
    grid = (mats, dw // TAIL_ROWS)
    row_spec = pl.BlockSpec((1, TAIL_ROWS, kv), lambda m, i, t: (m, i, 0))
    spec = pltpu.PrefetchScalarGridSpec(
        num_scalar_prefetch=1,
        grid=grid,
        in_specs=[
            row_spec,
            row_spec,
            pl.BlockSpec((1, TAIL_ROWS, rank), lambda m, i, t: (m, i, 0)),
            pl.BlockSpec((1, rank, kv), lambda m, i, t: (m, 0, 0)),
            pl.BlockSpec(memory_space=pl.ANY),
        ],
        out_specs=[row_spec, row_spec],
        scratch_shapes=[
            pltpu.VMEM((pieces, piece_rows, kv), jnp.float32),
            pltpu.VMEM((TAIL_ROWS, kv), jnp.float32),
            pltpu.SemaphoreType.DMA((pieces,)),
        ],
    )
    elems = mats * dw * kv
    cost = pl.CostEstimate(flops=2 * elems * rank, transcendentals=0, bytes_accessed=elems * (2 + 4 + 4 + 4 + 2))
    return pl.pallas_call(
        tail_kernel,
        grid_spec=spec,
        out_shape=[
            jax.ShapeDtypeStruct((mats, dw, kv), jnp.float32),
            jax.ShapeDtypeStruct((mats, dw, kv), jnp.bfloat16),
        ],
        cost_estimate=cost,
        compiler_params=pltpu.CompilerParams(
            dimension_semantics=("arbitrary", "arbitrary"), vmem_limit_bytes=48 * 1024 * 1024
        ),
    )(table, grads, errs, left_rows, right_t, carried)


def on_device(
    gradients,
    errors,
    warm_right,
    norm_grads,
    norm_weights,
    norm_moment,
    owners,
    slot_weights,
    slot_moment,
):
    dp_size = lax.axis_size("dp")
    group_size = lax.axis_size("group")
    replicas = dp_size * group_size
    rounds = radix4_rounds(dp_size, group_size)

    old_moment = slot_moment[0]
    carried = slot_weights[0].astype(jnp.float32) - (step_rate * momentum_decay) * old_moment

    merged = gradients[0].astype(jnp.float32) + errors[0]
    norm_local = norm_grads[0]
    warm_t = jnp.swapaxes(warm_right, 1, 2)
    left_list, right_list = [], []
    norm_sum = None
    for m in range(merged.shape[0]):
        part = merged[m : m + 1]
        p1 = left_t(part, warm_t[m : m + 1])
        flat = p1.reshape(-1)
        if m == 0:
            flat = jnp.concatenate([flat, norm_local.reshape(-1)])
        flat_sum = sum_all_to_all(flat, replicas)
        if m == 0:
            norm_sum = flat_sum[p1.size :].reshape(norm_local.shape)
            flat_sum, carried = lax.optimization_barrier((flat_sum, carried))
        p1_sum = flat_sum[: p1.size].reshape(p1.shape)
        lower_one = gram_factor(p1_sum)
        q1_sum = sum_radix4(right_t_of(part, p1_sum), rounds)
        right_one = solve_lower(lower_one, q1_sum) / replicas
        p2_sum = sum_all_to_all(left_t(part, right_one).reshape(-1), replicas).reshape(p1.shape)
        lower_two = gram_factor(p2_sum)
        left_list.append(solve_lower(lower_two, p2_sum))
        q2_sum = sum_radix4(right_t_of(part, p2_sum), rounds)
        right_list.append(solve_lower(lower_two, q2_sum) / replicas)
    left_two = jnp.concatenate(left_list)
    right_two = jnp.concatenate(right_list)
    every_carried = lax.all_gather(carried[None], ("dp", "group"), axis=0, tiled=True)
    new_norm_moment = momentum_decay * norm_moment + norm_sum / replicas
    new_norm_weights = norm_weights - step_rate * new_norm_moment
    piece_count = owners.shape[0]
    slot_count = slot_moment.shape[1]
    piece_rows = slot_moment.shape[2]
    features = slot_moment.shape[3]
    positions = jnp.arange(piece_count, dtype=jnp.int32)
    same_owner = owners[:, None] == owners[None, :]
    earlier = positions[:, None] < positions[None, :]
    slot_of = jnp.sum((same_owner & earlier).astype(jnp.int32), axis=0)
    my_index = lax.axis_index(("dp", "group"))
    owned = owners == my_index
    pieces_per_matrix = piece_count // merged.shape[0]
    moment_list = []
    for s in range(slot_count):
        hit = owned & (slot_of == s)
        piece = jnp.sum(jnp.where(hit, positions, 0))
        matrix = piece // pieces_per_matrix
        row0 = (piece % pieces_per_matrix) * piece_rows
        rows_l = lax.dynamic_slice(left_two, (matrix, 0, row0), (1, left_two.shape[1], piece_rows))[0]
        rows_r = lax.dynamic_index_in_dim(right_two, matrix, 0, keepdims=False)
        piece_update = jnp.einsum("rd,rk->dk", rows_l, rows_r, precision=MID)
        fresh = momentum_decay * old_moment[s] + piece_update
        moment_list.append(jnp.where(jnp.any(hit), fresh, old_moment[s]))
    moment_slots = jnp.stack(moment_list)
    table = jnp.clip(owners * slot_count + slot_of, 0, every_carried.shape[0] * slot_count - 1)
    carried_rows = every_carried.reshape(-1, piece_rows, features)
    new_errors, new_weights = tail(
        table, gradients[0], errors[0], jnp.swapaxes(left_two, 1, 2), right_two, carried_rows
    )
    new_errors = new_errors[None]
    return (new_errors, moment_slots[None], new_weights, new_norm_weights, new_norm_moment)


def solution(mesh):
    placed = (
        P(("dp", "group"), None, None, None),
        P(("dp", "group"), None, None, None),
        P(),
        P(("dp", "group"), None, None),
        P(),
        P(),
        P(),
        P(("dp", "group"), None, None, None),
        P(("dp", "group"), None, None, None),
    )
    return jax.shard_map(
        on_device,
        mesh=mesh,
        in_specs=placed,
        out_specs=(
            P(("dp", "group"), None, None, None),
            P(("dp", "group"), None, None, None),
            P(),
            P(),
            P(),
        ),
        check_vma=False,
    )
```

```python
import jax
import jax.numpy as jnp
from jax import lax
from jax.experimental import pallas as pl
from jax.experimental.pallas import tpu as pltpu
from jax.sharding import PartitionSpec as P

momentum_decay = 0.9
step_rate = 0.5
HI = lax.Precision.HIGHEST
MID = lax.Precision.HIGH


def radix4_rounds(dp_size, group_size):
    z_size = 4
    y_size = dp_size // (2 * z_size)

    def dp_of(y, z, c):
        return (y * z_size + z) * 2 + c

    rounds = [[("dp", [(i, i ^ 1) for i in range(dp_size)])]]
    rounds.append([("group", [(i, i ^ s) for i in range(group_size)]) for s in (1, 2, 3)])
    for along_z in (True, False):
        parts = []
        for s in (1, 2, 3):
            perm = []
            for y in range(y_size):
                for z in range(z_size):
                    for c in range(2):
                        dst = dp_of(y, z ^ s, c) if along_z else dp_of(y ^ s, z, c)
                        perm.append((dp_of(y, z, c), dst))
            parts.append(("dp", perm))
        rounds.append(parts)
    return rounds


def sum_radix4(x, rounds):
    for parts in rounds:
        if len(parts) == 1:
            x = x + lax.ppermute(x, parts[0][0], parts[0][1])
        else:
            r1, r2, r3 = [lax.ppermute(x, axis, perm) for axis, perm in parts]
            x = (x + r1) + (r2 + r3)
    return x


def sum_all_to_all(x, count):
    axes = ("dp", "group")
    rows = lax.all_to_all(x.reshape(count, -1), axes, 0, 0, tiled=False)
    mine = jnp.sum(rows, axis=0)
    spread = jnp.broadcast_to(mine[None], (count,) + mine.shape)
    return lax.all_to_all(spread, axes, 0, 0, tiled=False).reshape(-1)


def gram_factor(ft):
    gram = jnp.einsum("mrd,msd->mrs", ft, ft, precision=HI)
    return jnp.linalg.cholesky(gram)


def solve_lower(lower_factor, rows):
    return jax.scipy.linalg.solve_triangular(lower_factor, rows, lower=True)


def left_t(merged, right_t):
    return jnp.einsum("mdk,mrk->mrd", merged, right_t, precision=MID)


def right_t_of(merged, left_tr):
    return jnp.einsum("mdk,mrd->mrk", merged, left_tr, precision=MID)


TAIL_ROWS = 512


def tail_kernel(table, grads, errs, left_rows, right_t, carried, out_err, out_w, cbuf, ubuf, sems):
    m = pl.program_id(0)
    i = pl.program_id(1)
    pieces = cbuf.shape[0]
    piece_rows = cbuf.shape[1]
    blocks = pl.num_programs(1)
    per_block = out_w.shape[1] // piece_rows

    def piece_copy(j):
        return pltpu.make_async_copy(carried.at[table[j]], cbuf.at[j], sems.at[j])

    @pl.when((m == 0) & (i == 0))
    def _():
        def start(j, carry):
            piece_copy(j).start()
            return carry

        lax.fori_loop(0, pieces, start, 0)

    upd = jnp.dot(left_rows[0], right_t[0], precision=MID, preferred_element_type=jnp.float32)
    merged = grads[0].astype(jnp.float32) + errs[0]
    out_err[0] = merged - upd
    ubuf[...] = upd
    base = (m * blocks + i) * per_block

    def finish(p, carry):
        piece_copy(base + p).wait()
        rows = pl.ds(pl.multiple_of(p * piece_rows, piece_rows), piece_rows)
        out_w[0, rows, :] = (cbuf[base + p] - step_rate * ubuf[rows, :]).astype(out_w.dtype)
        return carry

    lax.fori_loop(0, per_block, finish, 0)


def tail(table, grads, errs, left_rows, right_t, carried):
    mats, dw, kv = grads.shape
    rank = left_rows.shape[2]
    piece_rows = carried.shape[1]
    pieces = mats * dw // piece_rows
    grid = (mats, dw // TAIL_ROWS)
    row_spec = pl.BlockSpec((1, TAIL_ROWS, kv), lambda m, i, t: (m, i, 0))
    spec = pltpu.PrefetchScalarGridSpec(
        num_scalar_prefetch=1,
        grid=grid,
        in_specs=[
            row_spec,
            row_spec,
            pl.BlockSpec((1, TAIL_ROWS, rank), lambda m, i, t: (m, i, 0)),
            pl.BlockSpec((1, rank, kv), lambda m, i, t: (m, 0, 0)),
            pl.BlockSpec(memory_space=pl.ANY),
        ],
        out_specs=[row_spec, row_spec],
        scratch_shapes=[
            pltpu.VMEM((pieces, piece_rows, kv), jnp.float32),
            pltpu.VMEM((TAIL_ROWS, kv), jnp.float32),
            pltpu.SemaphoreType.DMA((pieces,)),
        ],
    )
    elems = mats * dw * kv
    cost = pl.CostEstimate(flops=2 * elems * rank, transcendentals=0, bytes_accessed=elems * (2 + 4 + 4 + 4 + 2))
    return pl.pallas_call(
        tail_kernel,
        grid_spec=spec,
        out_shape=[
            jax.ShapeDtypeStruct((mats, dw, kv), jnp.float32),
            jax.ShapeDtypeStruct((mats, dw, kv), jnp.bfloat16),
        ],
        cost_estimate=cost,
        compiler_params=pltpu.CompilerParams(
            dimension_semantics=("arbitrary", "arbitrary"), vmem_limit_bytes=48 * 1024 * 1024
        ),
    )(table, grads, errs, left_rows, right_t, carried)


def on_device(
    gradients,
    errors,
    warm_right,
    norm_grads,
    norm_weights,
    norm_moment,
    owners,
    slot_weights,
    slot_moment,
):
    dp_size = lax.axis_size("dp")
    group_size = lax.axis_size("group")
    replicas = dp_size * group_size
    rounds = radix4_rounds(dp_size, group_size)

    old_moment = slot_moment[0]
    carried = slot_weights[0].astype(jnp.float32) - (step_rate * momentum_decay) * old_moment

    merged = gradients[0].astype(jnp.float32) + errors[0]
    lshape = (merged.shape[0], warm_right.shape[2], merged.shape[1])
    p1 = left_t(merged, jnp.swapaxes(warm_right, 1, 2))
    norm_local = norm_grads[0]
    joined = jnp.concatenate([p1.reshape(-1), norm_local.reshape(-1)])
    joined_sum = sum_all_to_all(joined, replicas)
    joined_sum, carried = lax.optimization_barrier((joined_sum, carried))
    every_carried = lax.all_gather(carried[None], ("dp", "group"), axis=0, tiled=True)
    p1_sum = joined_sum[: p1.size].reshape(lshape)
    norm_sum = joined_sum[p1.size :].reshape(norm_local.shape)
    lower_one = gram_factor(p1_sum)
    q1_sum = sum_radix4(right_t_of(merged, p1_sum), rounds)
    right_one = solve_lower(lower_one, q1_sum) / replicas
    p2_sum = sum_all_to_all(left_t(merged, right_one).reshape(-1), replicas).reshape(lshape)
    lower_two = gram_factor(p2_sum)
    left_two = solve_lower(lower_two, p2_sum)
    q2_sum = sum_radix4(right_t_of(merged, p2_sum), rounds)
    right_two = solve_lower(lower_two, q2_sum) / replicas
    new_norm_moment = momentum_decay * norm_moment + norm_sum / replicas
    new_norm_weights = norm_weights - step_rate * new_norm_moment
    piece_count = owners.shape[0]
    slot_count = slot_moment.shape[1]
    piece_rows = slot_moment.shape[2]
    features = slot_moment.shape[3]
    positions = jnp.arange(piece_count, dtype=jnp.int32)
    same_owner = owners[:, None] == owners[None, :]
    earlier = positions[:, None] < positions[None, :]
    slot_of = jnp.sum((same_owner & earlier).astype(jnp.int32), axis=0)
    my_index = lax.axis_index(("dp", "group"))
    owned = owners == my_index
    pieces_per_matrix = piece_count // merged.shape[0]
    moment_list = []
    for s in range(slot_count):
        hit = owned & (slot_of == s)
        piece = jnp.sum(jnp.where(hit, positions, 0))
        matrix = piece // pieces_per_matrix
        row0 = (piece % pieces_per_matrix) * piece_rows
        rows_l = lax.dynamic_slice(left_two, (matrix, 0, row0), (1, left_two.shape[1], piece_rows))[0]
        rows_r = lax.dynamic_index_in_dim(right_two, matrix, 0, keepdims=False)
        piece_update = jnp.einsum("rd,rk->dk", rows_l, rows_r, precision=MID)
        fresh = momentum_decay * old_moment[s] + piece_update
        moment_list.append(jnp.where(jnp.any(hit), fresh, old_moment[s]))
    moment_slots = jnp.stack(moment_list)
    table = jnp.clip(owners * slot_count + slot_of, 0, every_carried.shape[0] * slot_count - 1)
    carried_rows = every_carried.reshape(-1, piece_rows, features)
    new_errors, new_weights = tail(
        table, gradients[0], errors[0], jnp.swapaxes(left_two, 1, 2), right_two, carried_rows
    )
    new_errors = new_errors[None]
    return (new_errors, moment_slots[None], new_weights, new_norm_weights, new_norm_moment)


def solution(mesh):
    placed = (
        P(("dp", "group"), None, None, None),
        P(("dp", "group"), None, None, None),
        P(),
        P(("dp", "group"), None, None),
        P(),
        P(),
        P(),
        P(("dp", "group"), None, None, None),
        P(("dp", "group"), None, None, None),
    )
    return jax.shard_map(
        on_device,
        mesh=mesh,
        in_specs=placed,
        out_specs=(
            P(("dp", "group"), None, None, None),
            P(("dp", "group"), None, None, None),
            P(),
            P(),
            P(),
        ),
        check_vma=False,
    )
```

```python
import jax
import jax.numpy as jnp
from jax import lax
from jax.experimental import pallas as pl
from jax.experimental.pallas import tpu as pltpu
from jax.sharding import PartitionSpec as P

momentum_decay = 0.9
step_rate = 0.5
HI = lax.Precision.HIGHEST
MID = lax.Precision.HIGH


def radix4_rounds(dp_size, group_size):
    z_size = 4
    y_size = dp_size // (2 * z_size)

    def dp_of(y, z, c):
        return (y * z_size + z) * 2 + c

    rounds = [[("dp", [(i, i ^ 1) for i in range(dp_size)])]]
    rounds.append([("group", [(i, i ^ s) for i in range(group_size)]) for s in (1, 2, 3)])
    for along_z in (True, False):
        parts = []
        for s in (1, 2, 3):
            perm = []
            for y in range(y_size):
                for z in range(z_size):
                    for c in range(2):
                        dst = dp_of(y, z ^ s, c) if along_z else dp_of(y ^ s, z, c)
                        perm.append((dp_of(y, z, c), dst))
            parts.append(("dp", perm))
        rounds.append(parts)
    return rounds


def sum_radix4(x, rounds):
    for parts in rounds:
        if len(parts) == 1:
            x = x + lax.ppermute(x, parts[0][0], parts[0][1])
        else:
            r1, r2, r3 = [lax.ppermute(x, axis, perm) for axis, perm in parts]
            x = (x + r1) + (r2 + r3)
    return x


def sum_all_to_all(x, count):
    axes = ("dp", "group")
    rows = lax.all_to_all(x.reshape(count, -1), axes, 0, 0, tiled=False)
    mine = jnp.sum(rows, axis=0)
    spread = jnp.broadcast_to(mine[None], (count,) + mine.shape)
    return lax.all_to_all(spread, axes, 0, 0, tiled=False).reshape(-1)


def gram_factor(ft):
    gram = jnp.einsum("mrd,msd->mrs", ft, ft, precision=HI)
    return jnp.linalg.cholesky(gram)


def solve_lower(lower_factor, rows):
    return jax.scipy.linalg.solve_triangular(lower_factor, rows, lower=True)


def left_t(merged, right_t):
    return jnp.einsum("mdk,mrk->mrd", merged, right_t, precision=MID)


def right_t_of(merged, left_tr):
    return jnp.einsum("mdk,mrd->mrk", merged, left_tr, precision=MID)


TAIL_ROWS = 1024


def tail_kernel(table, grads, errs, left_rows, right_t, carried, out_err, out_w, cbuf, ubuf, sems):
    m = pl.program_id(0)
    i = pl.program_id(1)
    pieces = cbuf.shape[0]
    piece_rows = cbuf.shape[1]
    blocks = pl.num_programs(1)
    per_block = out_w.shape[1] // piece_rows

    def piece_copy(j):
        return pltpu.make_async_copy(carried.at[table[j]], cbuf.at[j], sems.at[j])

    @pl.when((m == 0) & (i == 0))
    def _():
        def start(j, carry):
            piece_copy(j).start()
            return carry

        lax.fori_loop(0, pieces, start, 0)

    upd = jnp.dot(left_rows[0], right_t[0], precision=MID, preferred_element_type=jnp.float32)
    merged = grads[0].astype(jnp.float32) + errs[0]
    out_err[0] = merged - upd
    ubuf[...] = upd
    base = (m * blocks + i) * per_block

    def finish(p, carry):
        piece_copy(base + p).wait()
        rows = pl.ds(pl.multiple_of(p * piece_rows, piece_rows), piece_rows)
        out_w[0, rows, :] = (cbuf[base + p] - step_rate * ubuf[rows, :]).astype(out_w.dtype)
        return carry

    lax.fori_loop(0, per_block, finish, 0)


def tail(table, grads, errs, left_rows, right_t, carried):
    mats, dw, kv = grads.shape
    rank = left_rows.shape[2]
    piece_rows = carried.shape[1]
    pieces = mats * dw // piece_rows
    grid = (mats, dw // TAIL_ROWS)
    row_spec = pl.BlockSpec((1, TAIL_ROWS, kv), lambda m, i, t: (m, i, 0))
    spec = pltpu.PrefetchScalarGridSpec(
        num_scalar_prefetch=1,
        grid=grid,
        in_specs=[
            row_spec,
            row_spec,
            pl.BlockSpec((1, TAIL_ROWS, rank), lambda m, i, t: (m, i, 0)),
            pl.BlockSpec((1, rank, kv), lambda m, i, t: (m, 0, 0)),
            pl.BlockSpec(memory_space=pl.ANY),
        ],
        out_specs=[row_spec, row_spec],
        scratch_shapes=[
            pltpu.VMEM((pieces, piece_rows, kv), jnp.float32),
            pltpu.VMEM((TAIL_ROWS, kv), jnp.float32),
            pltpu.SemaphoreType.DMA((pieces,)),
        ],
    )
    elems = mats * dw * kv
    cost = pl.CostEstimate(flops=2 * elems * rank, transcendentals=0, bytes_accessed=elems * (2 + 4 + 4 + 4 + 2))
    return pl.pallas_call(
        tail_kernel,
        grid_spec=spec,
        out_shape=[
            jax.ShapeDtypeStruct((mats, dw, kv), jnp.float32),
            jax.ShapeDtypeStruct((mats, dw, kv), jnp.bfloat16),
        ],
        cost_estimate=cost,
        compiler_params=pltpu.CompilerParams(
            dimension_semantics=("arbitrary", "arbitrary"), vmem_limit_bytes=48 * 1024 * 1024
        ),
    )(table, grads, errs, left_rows, right_t, carried)


def on_device(
    gradients,
    errors,
    warm_right,
    norm_grads,
    norm_weights,
    norm_moment,
    owners,
    slot_weights,
    slot_moment,
):
    dp_size = lax.axis_size("dp")
    group_size = lax.axis_size("group")
    replicas = dp_size * group_size
    rounds = radix4_rounds(dp_size, group_size)

    old_moment = slot_moment[0]
    carried = slot_weights[0].astype(jnp.float32) - (step_rate * momentum_decay) * old_moment

    merged = gradients[0].astype(jnp.float32) + errors[0]
    lshape = (merged.shape[0], warm_right.shape[2], merged.shape[1])
    p1 = left_t(merged, jnp.swapaxes(warm_right, 1, 2))
    norm_local = norm_grads[0]
    joined = jnp.concatenate([p1.reshape(-1), norm_local.reshape(-1)])
    joined_sum = sum_all_to_all(joined, replicas)
    joined_sum, carried = lax.optimization_barrier((joined_sum, carried))
    every_carried = lax.all_gather(carried[None], ("dp", "group"), axis=0, tiled=True)
    p1_sum = joined_sum[: p1.size].reshape(lshape)
    norm_sum = joined_sum[p1.size :].reshape(norm_local.shape)
    lower_one = gram_factor(p1_sum)
    q1_sum = sum_radix4(right_t_of(merged, p1_sum), rounds)
    right_one = solve_lower(lower_one, q1_sum) / replicas
    p2_sum = sum_all_to_all(left_t(merged, right_one).reshape(-1), replicas).reshape(lshape)
    lower_two = gram_factor(p2_sum)
    left_two = solve_lower(lower_two, p2_sum)
    q2_sum = sum_radix4(right_t_of(merged, p2_sum), rounds)
    right_two = solve_lower(lower_two, q2_sum) / replicas
    new_norm_moment = momentum_decay * norm_moment + norm_sum / replicas
    new_norm_weights = norm_weights - step_rate * new_norm_moment
    piece_count = owners.shape[0]
    slot_count = slot_moment.shape[1]
    piece_rows = slot_moment.shape[2]
    features = slot_moment.shape[3]
    positions = jnp.arange(piece_count, dtype=jnp.int32)
    same_owner = owners[:, None] == owners[None, :]
    earlier = positions[:, None] < positions[None, :]
    slot_of = jnp.sum((same_owner & earlier).astype(jnp.int32), axis=0)
    my_index = lax.axis_index(("dp", "group"))
    owned = owners == my_index
    pieces_per_matrix = piece_count // merged.shape[0]
    moment_list = []
    for s in range(slot_count):
        hit = owned & (slot_of == s)
        piece = jnp.sum(jnp.where(hit, positions, 0))
        matrix = piece // pieces_per_matrix
        row0 = (piece % pieces_per_matrix) * piece_rows
        rows_l = lax.dynamic_slice(left_two, (matrix, 0, row0), (1, left_two.shape[1], piece_rows))[0]
        rows_r = lax.dynamic_index_in_dim(right_two, matrix, 0, keepdims=False)
        piece_update = jnp.einsum("rd,rk->dk", rows_l, rows_r, precision=MID)
        fresh = momentum_decay * old_moment[s] + piece_update
        moment_list.append(jnp.where(jnp.any(hit), fresh, old_moment[s]))
    moment_slots = jnp.stack(moment_list)
    table = jnp.clip(owners * slot_count + slot_of, 0, every_carried.shape[0] * slot_count - 1)
    carried_rows = every_carried.reshape(-1, piece_rows, features)
    new_errors, new_weights = tail(
        table, gradients[0], errors[0], jnp.swapaxes(left_two, 1, 2), right_two, carried_rows
    )
    new_errors = new_errors[None]
    return (new_errors, moment_slots[None], new_weights, new_norm_weights, new_norm_moment)


def solution(mesh):
    placed = (
        P(("dp", "group"), None, None, None),
        P(("dp", "group"), None, None, None),
        P(),
        P(("dp", "group"), None, None),
        P(),
        P(),
        P(),
        P(("dp", "group"), None, None, None),
        P(("dp", "group"), None, None, None),
    )
    return jax.shard_map(
        on_device,
        mesh=mesh,
        in_specs=placed,
        out_specs=(
            P(("dp", "group"), None, None, None),
            P(("dp", "group"), None, None, None),
            P(),
            P(),
            P(),
        ),
        check_vma=False,
    )
```

```python
import jax
import jax.numpy as jnp
from jax import lax
from jax.experimental import pallas as pl
from jax.experimental.pallas import tpu as pltpu
from jax.sharding import PartitionSpec as P

momentum_decay = 0.9
step_rate = 0.5
HI = lax.Precision.HIGHEST
MID = lax.Precision.HIGH


def radix4_rounds(dp_size, group_size):
    z_size = 4
    y_size = dp_size // (2 * z_size)

    def dp_of(y, z, c):
        return (y * z_size + z) * 2 + c

    rounds = [[("dp", [(i, i ^ 1) for i in range(dp_size)])]]
    rounds.append([("group", [(i, i ^ s) for i in range(group_size)]) for s in (1, 2, 3)])
    for along_z in (True, False):
        parts = []
        for s in (1, 2, 3):
            perm = []
            for y in range(y_size):
                for z in range(z_size):
                    for c in range(2):
                        dst = dp_of(y, z ^ s, c) if along_z else dp_of(y ^ s, z, c)
                        perm.append((dp_of(y, z, c), dst))
            parts.append(("dp", perm))
        rounds.append(parts)
    return rounds


def sum_radix4(x, rounds):
    for parts in rounds:
        if len(parts) == 1:
            x = x + lax.ppermute(x, parts[0][0], parts[0][1])
        else:
            r1, r2, r3 = [lax.ppermute(x, axis, perm) for axis, perm in parts]
            x = (x + r1) + (r2 + r3)
    return x


def sum_all_to_all(x, count):
    axes = ("dp", "group")
    rows = lax.all_to_all(x.reshape(count, -1), axes, 0, 0, tiled=False)
    mine = jnp.sum(rows, axis=0)
    spread = jnp.broadcast_to(mine[None], (count,) + mine.shape)
    return lax.all_to_all(spread, axes, 0, 0, tiled=False).reshape(-1)


def gram_factor(ft):
    gram = jnp.einsum("mrd,msd->mrs", ft, ft, precision=HI)
    return jnp.linalg.cholesky(gram)


def solve_lower(lower_factor, rows):
    return jax.scipy.linalg.solve_triangular(lower_factor, rows, lower=True)


def left_t(merged, right_t):
    return jnp.einsum("mdk,mrk->mrd", merged, right_t, precision=MID)


def right_t_of(merged, left_tr):
    return jnp.einsum("mdk,mrd->mrk", merged, left_tr, precision=MID)


TAIL_ROWS = 2048


def tail_kernel(table, grads, errs, left_rows, right_t, carried, out_err, out_w, cbuf, ubuf, sems):
    m = pl.program_id(0)
    i = pl.program_id(1)
    pieces = cbuf.shape[0]
    piece_rows = cbuf.shape[1]
    blocks = pl.num_programs(1)
    per_block = out_w.shape[1] // piece_rows

    def piece_copy(j):
        return pltpu.make_async_copy(carried.at[table[j]], cbuf.at[j], sems.at[j])

    @pl.when((m == 0) & (i == 0))
    def _():
        def start(j, carry):
            piece_copy(j).start()
            return carry

        lax.fori_loop(0, pieces, start, 0)

    upd = jnp.dot(left_rows[0], right_t[0], precision=MID, preferred_element_type=jnp.float32)
    merged = grads[0].astype(jnp.float32) + errs[0]
    out_err[0] = merged - upd
    ubuf[...] = upd
    base = (m * blocks + i) * per_block

    def finish(p, carry):
        piece_copy(base + p).wait()
        rows = pl.ds(pl.multiple_of(p * piece_rows, piece_rows), piece_rows)
        out_w[0, rows, :] = (cbuf[base + p] - step_rate * ubuf[rows, :]).astype(out_w.dtype)
        return carry

    lax.fori_loop(0, per_block, finish, 0)


def tail(table, grads, errs, left_rows, right_t, carried):
    mats, dw, kv = grads.shape
    rank = left_rows.shape[2]
    piece_rows = carried.shape[1]
    pieces = mats * dw // piece_rows
    grid = (mats, dw // TAIL_ROWS)
    row_spec = pl.BlockSpec((1, TAIL_ROWS, kv), lambda m, i, t: (m, i, 0))
    spec = pltpu.PrefetchScalarGridSpec(
        num_scalar_prefetch=1,
        grid=grid,
        in_specs=[
            row_spec,
            row_spec,
            pl.BlockSpec((1, TAIL_ROWS, rank), lambda m, i, t: (m, i, 0)),
            pl.BlockSpec((1, rank, kv), lambda m, i, t: (m, 0, 0)),
            pl.BlockSpec(memory_space=pl.ANY),
        ],
        out_specs=[row_spec, row_spec],
        scratch_shapes=[
            pltpu.VMEM((pieces, piece_rows, kv), jnp.float32),
            pltpu.VMEM((TAIL_ROWS, kv), jnp.float32),
            pltpu.SemaphoreType.DMA((pieces,)),
        ],
    )
    elems = mats * dw * kv
    cost = pl.CostEstimate(flops=2 * elems * rank, transcendentals=0, bytes_accessed=elems * (2 + 4 + 4 + 4 + 2))
    return pl.pallas_call(
        tail_kernel,
        grid_spec=spec,
        out_shape=[
            jax.ShapeDtypeStruct((mats, dw, kv), jnp.float32),
            jax.ShapeDtypeStruct((mats, dw, kv), jnp.bfloat16),
        ],
        cost_estimate=cost,
        compiler_params=pltpu.CompilerParams(
            dimension_semantics=("arbitrary", "arbitrary"), vmem_limit_bytes=56 * 1024 * 1024
        ),
    )(table, grads, errs, left_rows, right_t, carried)


def on_device(
    gradients,
    errors,
    warm_right,
    norm_grads,
    norm_weights,
    norm_moment,
    owners,
    slot_weights,
    slot_moment,
):
    dp_size = lax.axis_size("dp")
    group_size = lax.axis_size("group")
    replicas = dp_size * group_size
    rounds = radix4_rounds(dp_size, group_size)

    old_moment = slot_moment[0]
    carried = slot_weights[0].astype(jnp.float32) - (step_rate * momentum_decay) * old_moment

    merged = gradients[0].astype(jnp.float32) + errors[0]
    lshape = (merged.shape[0], warm_right.shape[2], merged.shape[1])
    p1 = left_t(merged, jnp.swapaxes(warm_right, 1, 2))
    norm_local = norm_grads[0]
    joined = jnp.concatenate([p1.reshape(-1), norm_local.reshape(-1)])
    joined_sum = sum_all_to_all(joined, replicas)
    joined_sum, carried = lax.optimization_barrier((joined_sum, carried))
    every_carried = lax.all_gather(carried[None], ("dp", "group"), axis=0, tiled=True)
    p1_sum = joined_sum[: p1.size].reshape(lshape)
    norm_sum = joined_sum[p1.size :].reshape(norm_local.shape)
    lower_one = gram_factor(p1_sum)
    q1_sum = sum_radix4(right_t_of(merged, p1_sum), rounds)
    right_one = solve_lower(lower_one, q1_sum) / replicas
    p2_sum = sum_all_to_all(left_t(merged, right_one).reshape(-1), replicas).reshape(lshape)
    lower_two = gram_factor(p2_sum)
    left_two = solve_lower(lower_two, p2_sum)
    q2_sum = sum_radix4(right_t_of(merged, p2_sum), rounds)
    right_two = solve_lower(lower_two, q2_sum) / replicas
    new_norm_moment = momentum_decay * norm_moment + norm_sum / replicas
    new_norm_weights = norm_weights - step_rate * new_norm_moment
    piece_count = owners.shape[0]
    slot_count = slot_moment.shape[1]
    piece_rows = slot_moment.shape[2]
    features = slot_moment.shape[3]
    positions = jnp.arange(piece_count, dtype=jnp.int32)
    same_owner = owners[:, None] == owners[None, :]
    earlier = positions[:, None] < positions[None, :]
    slot_of = jnp.sum((same_owner & earlier).astype(jnp.int32), axis=0)
    my_index = lax.axis_index(("dp", "group"))
    owned = owners == my_index
    pieces_per_matrix = piece_count // merged.shape[0]
    moment_list = []
    for s in range(slot_count):
        hit = owned & (slot_of == s)
        piece = jnp.sum(jnp.where(hit, positions, 0))
        matrix = piece // pieces_per_matrix
        row0 = (piece % pieces_per_matrix) * piece_rows
        rows_l = lax.dynamic_slice(left_two, (matrix, 0, row0), (1, left_two.shape[1], piece_rows))[0]
        rows_r = lax.dynamic_index_in_dim(right_two, matrix, 0, keepdims=False)
        piece_update = jnp.einsum("rd,rk->dk", rows_l, rows_r, precision=MID)
        fresh = momentum_decay * old_moment[s] + piece_update
        moment_list.append(jnp.where(jnp.any(hit), fresh, old_moment[s]))
    moment_slots = jnp.stack(moment_list)
    table = jnp.clip(owners * slot_count + slot_of, 0, every_carried.shape[0] * slot_count - 1)
    carried_rows = every_carried.reshape(-1, piece_rows, features)
    new_errors, new_weights = tail(
        table, gradients[0], errors[0], jnp.swapaxes(left_two, 1, 2), right_two, carried_rows
    )
    new_errors = new_errors[None]
    return (new_errors, moment_slots[None], new_weights, new_norm_weights, new_norm_moment)


def solution(mesh):
    placed = (
        P(("dp", "group"), None, None, None),
        P(("dp", "group"), None, None, None),
        P(),
        P(("dp", "group"), None, None),
        P(),
        P(),
        P(),
        P(("dp", "group"), None, None, None),
        P(("dp", "group"), None, None, None),
    )
    return jax.shard_map(
        on_device,
        mesh=mesh,
        in_specs=placed,
        out_specs=(
            P(("dp", "group"), None, None, None),
            P(("dp", "group"), None, None, None),
            P(),
            P(),
            P(),
        ),
        check_vma=False,
    )
```
